512 devices in a mesh: gx: 16 (over z, core), gy: 32 (over y, x).
Axes of the slice: x: 4, y: 8, z: 8, core: 2. Of those that a mesh axis runs over, the one named last changes fastest.
Arguments:
- stencil: float32 [32, 64, 2, 32, 864], P('gx', 'gy'), may hold values from -0.21875 to 0.21875
- pattern: int32 [32, 64, 2, 27], P('gx', 'gy'), may hold values 0 or 1
- tentative: float32 [32, 64, 2, 32, 32], P('gx', 'gy'), may hold values from -1 to 1
- diag_inverse: float32 [32, 64, 2, 32, 32], P('gx', 'gy'), may hold values from -1 to 1
- coarse_pattern: int32 [16, 32, 9], P('gx', 'gy'), may hold values 0 or 1
- slot: int32 [16, 32], P('gx', 'gy'), may hold values from 0 to 3, as said below
Outputs:
- coarse_rows: float32 [16, 32, 32, 288], P('gx', 'gy')
- grouped: float32 [16, 32, 4, 32, 288], P('gx', 'gy')
The draws below stay inside these ranges and needn't reach their ends.
Inputs may be any that keep to these rules, and one draw needn't show every extreme that they name: For each y, the four entries slot[4 g .. 4 g + 3, y] are 0, 1, 2, 3 in some order.
All inputs are finite; a program needn't handle non-finite values. No bound on the sum of `pattern` or of `coarse_pattern` on one device may be relied on, other than what follows from the above.
Results may differ from the reference program's by a relative error of at most 0.0003.
Values sent between devices are 32-bit elements; how exact they have to be, the bound alone decides.
No kernel may reach another device: no remote copies, remote signals or barrier semaphores. Data moves between devices by JAX's collectives and lax.ppermute only.
A program may use at most 64 MiB of HBM per device.

```python
import jax
import jax.numpy as jnp
import numpy as np
from jax import lax

B = 32
FX = 32
FY = 64
N_GX = 16
N_GY = 32


def one_permutation(subkey):
    return jax.random.permutation(subkey, 4)


def draw_slot(key, part):
    groups = N_GX // 4 * N_GY
    subkeys = jax.random.split(key, groups)
    orders = jax.vmap(one_permutation)(subkeys)
    orders = orders.reshape(N_GX // 4, N_GY, 4)
    return jnp.transpose(orders, (0, 2, 1)).reshape(N_GX, N_GY).astype(jnp.int32)


def with_ends(array, key, least, high):
    longest = array.shape.index(max(array.shape))
    spots = []
    for shift in (0, 1):
        where = [jax.random.randint(jax.random.fold_in(key, axis), (), 0, length) for axis, length in enumerate(array.shape)]
        where[longest] = (where[longest] + shift) % array.shape[longest]
        spots.append(tuple(where))
    return array.at[spots[0]].set(least).at[spots[1]].set(high)


def shard_levels(rng, shape, cuts, smallest, top_value):
    def one(dim, shards_of):
        heights = jax.random.uniform(jax.random.fold_in(jax.random.fold_in(rng, 6), dim), (shards_of,), jnp.float32, smallest / len(cuts), top_value / len(cuts))
        return jnp.repeat(jnp.exp(heights), shape[dim] // shards_of).reshape((-1,) + (1,) * (len(shape) - dim - 1))

    gain = one(*cuts[0])
    for cut in cuts[1:]:
        gain = gain * one(*cut)
    return gain


def noise(own_key, extent, scale, limit, cuts=(), kind=jnp.bfloat16):
    array = scale * jax.random.normal(own_key, extent, jnp.float32)
    if cuts:
        array = array * shard_levels(own_key, extent, cuts, -0.22, 0.18)
    return jnp.clip(array, -limit, limit).astype(kind)


def setup_inputs(seed: int = 0) -> dict:
    key_of = jax.random.split(jax.random.key(seed), 7)
    stencil = noise(key_of[0], (FX, FY, 2, B, 27 * B), (27 * B) ** -0.5, 0.21875, ((0, 16), (1, 32)), jnp.float32)
    pattern = with_ends((jax.random.randint(key_of[1], (FX, FY, 2, 27), 0, 4) < 3).astype(jnp.int32), jax.random.fold_in(key_of[1], 1), 0, 1)
    tentative = noise(key_of[2], (FX, FY, 2, B, B), B ** -0.5, 1.0, ((0, 16), (1, 32)), jnp.float32)
    diag_inverse = noise(key_of[3], (FX, FY, 2, B, B), B ** -0.5, 1.0, ((0, 16), (1, 32)), jnp.float32)
    coarse_pattern = with_ends((jax.random.randint(key_of[4], (N_GX, N_GY, 9), 0, 4) < 3).astype(jnp.int32), jax.random.fold_in(key_of[4], 1), 0, 1)
    slot = draw_slot(jax.random.fold_in(key_of[6], 71), 0)
    return dict(stencil=stencil, pattern=pattern, tentative=tentative, diag_inverse=diag_inverse, coarse_pattern=coarse_pattern, slot=slot)


OMEGA = 0.6


def offset_list():
    result = []
    for shift_x in (-1, 0, 1):
        for shift_y in (-1, 0, 1):
            for shift_z in (-1, 0, 1):
                result.append((shift_x, shift_y, shift_z))
    return result


def channel_table():
    table = np.zeros((2, 2, 2, 27, 9), np.float32)
    for cell_x in range(2):
        for cell_y in range(2):
            for cell_z in range(2):
                for number, offset in enumerate(offset_list()):
                    reach_x = (cell_x + offset[0]) // 2
                    reach_y = (cell_y + offset[1]) // 2
                    table[cell_x, cell_y, cell_z, number, 3 * (reach_x + 1) + (reach_y + 1)] = 1.0
    return table


def prolong(stencil_rows, tent_pad, inverse_diag):
    width = tent_pad.shape[-1]
    slabs = []
    for offset in offset_list():
        slabs.append(tent_pad[1 + offset[0]:3 + offset[0], 1 + offset[1]:3 + offset[1], 1 + offset[2]:3 + offset[2]])
    neighbours = jnp.stack(slabs, axis=3)
    blocks = stencil_rows.reshape(2, 2, 2, width, 27, width)
    coupled = jnp.einsum("xyzrok,xyzokm->xyzorm", blocks, neighbours, precision=lax.Precision.HIGHEST)
    table = jnp.asarray(channel_table(), jnp.float32)
    placed = jnp.einsum("xyzorm,xyzoc->xyzrcm", coupled, table, precision=lax.Precision.HIGHEST)
    smoothed = jnp.einsum("xyzrs,xyzscm->xyzrcm", inverse_diag, placed, precision=lax.Precision.HIGHEST)
    centre = jnp.asarray(np.eye(9, dtype=np.float32)[4], jnp.float32)
    own_block = tent_pad[1:3, 1:3, 1:3]
    result = own_block[:, :, :, :, None, :] * centre[:, None] - OMEGA * smoothed
    return result.reshape(2, 2, 2, width, 9 * width)


def region_shift(position):
    if position == 0:
        return -1
    if position == 3:
        return 1
    return 0


def shift_channels(block, shift_x, shift_y):
    depth, width = block.shape[0], block.shape[1]
    channel_grid = block.reshape(depth, width, 3, 3, width)
    channel_grid = jnp.pad(channel_grid, ((0, 0), (0, 0), (1, 1), (1, 1), (0, 0)))
    channel_grid = channel_grid[:, :, 1 - shift_x:4 - shift_x, 1 - shift_y:4 - shift_y, :]
    return channel_grid.reshape(depth, width, 9 * width)


def to_frame(padded):
    lines = []
    for pos_x in range(4):
        column = []
        for pos_y in range(4):
            column.append(shift_channels(padded[pos_x, pos_y], region_shift(pos_x), region_shift(pos_y)))
        lines.append(jnp.stack(column))
    return jnp.stack(lines)


def galerkin(stencil_rows, frame, prolong_own):
    width = prolong_own.shape[3]
    frame_pad = jnp.pad(frame, ((0, 0), (0, 0), (1, 1), (0, 0), (0, 0)))
    applied = []
    for cell_x in range(2):
        for cell_y in range(2):
            for cell_z in range(2):
                pieces = []
                for offset in offset_list():
                    pieces.append(frame_pad[1 + cell_x + offset[0], 1 + cell_y + offset[1], 1 + cell_z + offset[2]])
                stacked = jnp.concatenate(pieces, axis=0)
                applied.append(jnp.dot(stencil_rows[cell_x, cell_y, cell_z], stacked, precision=lax.Precision.HIGHEST))
    applied = jnp.concatenate(applied, axis=0)
    left_side = prolong_own.reshape(8 * width, 9 * width)
    full_product = lax.dot_general(left_side, applied, (((0,), (0,)), ((), ())), precision=lax.Precision.HIGHEST)
    full_product = full_product.reshape(3, 3, width, 3, 3, width)
    full_product = jnp.pad(full_product, ((0, 0), (0, 0), (0, 0), (1, 1), (1, 1), (0, 0)))
    lines = []
    for row_x in range(3):
        column = []
        for row_y in range(3):
            piece = full_product[row_x, row_y, :, row_x:row_x + 3, row_y:row_y + 3, :]
            column.append(piece.reshape(width, 9 * width))
        lines.append(jnp.stack(column))
    return jnp.stack(lines)


def reference(stencil, pattern, tentative, diag_inverse, coarse_pattern, slot):
    width = tentative.shape[-1]
    keep_mask = jnp.repeat(pattern.astype(jnp.float32), width, axis=-1)[:, :, :, None, :]
    stencil_rows = stencil * keep_mask
    tent_pad = jnp.pad(tentative, ((1, 1), (1, 1), (1, 1), (0, 0), (0, 0)))
    flat_index = jnp.arange(N_GX * N_GY, dtype=jnp.int32)

    def make_prolong(number):
        agg_x = (number // N_GY).astype(jnp.int32)
        agg_y = (number % N_GY).astype(jnp.int32)
        anchor = agg_x * 0
        own_rows = lax.dynamic_slice(stencil_rows, (2 * agg_x, 2 * agg_y, anchor, anchor, anchor), (2, 2, 2, width, 27 * width))
        near_tent = lax.dynamic_slice(tent_pad, (2 * agg_x, 2 * agg_y, anchor, anchor, anchor), (4, 4, 4, width, width))
        own_inverse = lax.dynamic_slice(diag_inverse, (2 * agg_x, 2 * agg_y, anchor, anchor, anchor), (2, 2, 2, width, width))
        return prolong(own_rows, near_tent, own_inverse)

    prolongs = lax.map(make_prolong, flat_index)
    prolongs = prolongs.reshape(N_GX, N_GY, 2, 2, 2, width, 9 * width)
    cell_field = prolongs.transpose(0, 2, 1, 3, 4, 5, 6).reshape(FX, FY, 2, width, 9 * width)
    cell_pad = jnp.pad(cell_field, ((1, 1), (1, 1), (0, 0), (0, 0), (0, 0)))

    def make_partial(number):
        agg_x = (number // N_GY).astype(jnp.int32)
        agg_y = (number % N_GY).astype(jnp.int32)
        anchor = agg_x * 0
        own_rows = lax.dynamic_slice(stencil_rows, (2 * agg_x, 2 * agg_y, anchor, anchor, anchor), (2, 2, 2, width, 27 * width))
        near_cells = lax.dynamic_slice(cell_pad, (2 * agg_x, 2 * agg_y, anchor, anchor, anchor), (4, 4, 2, width, 9 * width))
        own_cells = lax.dynamic_slice(cell_field, (2 * agg_x, 2 * agg_y, anchor, anchor, anchor), (2, 2, 2, width, 9 * width))
        return galerkin(own_rows, to_frame(near_cells), own_cells)

    partials = lax.map(make_partial, flat_index).reshape(N_GX, N_GY, 3, 3, width, 9 * width)
    partial_pad = jnp.pad(partials, ((1, 1), (1, 1), (0, 0), (0, 0), (0, 0), (0, 0)))
    total = jnp.zeros((N_GX, N_GY, width, 9 * width), jnp.float32)
    for shift_x in (-1, 0, 1):
        for shift_y in (-1, 0, 1):
            total = total + partial_pad[1 + shift_x:1 + shift_x + N_GX, 1 + shift_y:1 + shift_y + N_GY, 1 - shift_x, 1 - shift_y]
    column_mask = jnp.repeat(coarse_pattern.astype(jnp.float32), width, axis=-1)[:, :, None, :]
    coarse_rows = total * column_mask
    members = coarse_rows.reshape(N_GX // 4, 4, N_GY, width, 9 * width)
    member_slots = slot.reshape(N_GX // 4, 4, N_GY)
    choose = (member_slots[..., None] == jnp.arange(4, dtype=jnp.int32)).astype(jnp.float32)
    selected = jnp.einsum("gjyrm,gjys->gysrm", members, choose, precision=lax.Precision.HIGHEST)
    grouped = jnp.repeat(selected[:, None], 4, axis=1).reshape(N_GX, N_GY, 4, width, 9 * width)
    return coarse_rows, grouped
```

```python
import jax
import jax.numpy as jnp
import numpy as np
from jax import lax
from jax.sharding import PartitionSpec as P

OMEGA = 0.6
HI = lax.Precision.HIGHEST


def shift(block, axis, forward):
    count = lax.axis_size(axis)
    if forward:
        pairs = [(i, i + 1) for i in range(count - 1)]
    else:
        pairs = [(i + 1, i) for i in range(count - 1)]
    return lax.ppermute(block, axis, pairs)


def to_positions(rows):
    width = rows.shape[3]
    grid = rows.reshape(2, 2, 2, width, 3, 3, 3, -1)
    cells = []
    for cell_x in range(2):
        for cell_y in range(2):
            for cell_z in range(2):
                block = grid[cell_x, cell_y, cell_z]
                block = block[:, :, :, 1:3] if cell_z == 0 else block[:, :, :, 0:2]
                zeros_x = jnp.zeros_like(block[:, :1])
                block = jnp.concatenate([block, zeros_x] if cell_x == 0 else [zeros_x, block], axis=1)
                zeros_y = jnp.zeros_like(block[:, :, :1])
                block = jnp.concatenate([block, zeros_y] if cell_y == 0 else [zeros_y, block], axis=2)
                cells.append(block)
    return jnp.stack(cells).reshape(2, 2, 2, width, 4, 4, 2, -1)


def reach_mask():
    reach = [0, 1, 1, 2]
    table = np.zeros((4, 4, 3, 3), np.float32)
    for pos_x in range(4):
        for pos_y in range(4):
            table[pos_x, pos_y, reach[pos_x], reach[pos_y]] = 1.0
    return table


def local(stencil, pattern, tentative, diag_inverse, coarse_pattern, slot):
    width = tentative.shape[-1]
    keep_mask = jnp.repeat(pattern.astype(jnp.float32), width, axis=-1)[:, :, :, None, :]
    stencil_rows = stencil * keep_mask
    scaled_rows = jnp.einsum("xyzrs,xyzsk->xyzrk", diag_inverse, stencil_rows, precision=HI)
    both = to_positions(jnp.concatenate([stencil_rows, scaled_rows], axis=3))
    stencil_pos = both[:, :, :, :width].reshape(8 * width, 32 * width)
    scaled_pos = both[:, :, :, width:].reshape(8 * width, 32 * width)

    left = shift(tentative[1], "gx", True)
    right = shift(tentative[0], "gx", False)
    tent_x = jnp.concatenate([left[None], tentative, right[None]], axis=0)
    low = shift(tent_x[:, 1], "gy", True)
    high = shift(tent_x[:, 0], "gy", False)
    tent_frame = jnp.concatenate([low[:, None], tent_x, high[:, None]], axis=1)

    mask = jnp.asarray(reach_mask())
    tent_agg = tent_frame[:, :, :, :, None, None, :] * mask[:, :, None, None, :, :, None]
    smoothed = jnp.dot(scaled_pos, tent_agg.reshape(32 * width, 9 * width), precision=HI)
    centre = jnp.asarray(np.eye(9, dtype=np.float32)[4])
    own_tent = tentative.reshape(8 * width, 1, width) * centre[None, :, None]
    prolong_own = own_tent.reshape(8 * width, 9 * width) - OMEGA * smoothed

    grid = prolong_own.reshape(2, 2, 2, width, 3, 3, width)
    from_right = shift(grid[0, :, :, :, 0:2], "gx", False)
    from_left = shift(grid[1, :, :, :, 1:3], "gx", True)
    pad_x_low = ((0, 0), (0, 0), (0, 0), (0, 1), (0, 0), (0, 0))
    pad_x_high = ((0, 0), (0, 0), (0, 0), (1, 0), (0, 0), (0, 0))
    prolong_x = jnp.concatenate(
        [jnp.pad(from_left, pad_x_low)[None], grid, jnp.pad(from_right, pad_x_high)[None]], axis=0
    )
    from_high = shift(prolong_x[:, 0, :, :, :, 0:2], "gy", False)
    from_low = shift(prolong_x[:, 1, :, :, :, 1:3], "gy", True)
    pad_y_low = ((0, 0), (0, 0), (0, 0), (0, 0), (0, 1), (0, 0))
    pad_y_high = ((0, 0), (0, 0), (0, 0), (0, 0), (1, 0), (0, 0))
    prolong_frame = jnp.concatenate(
        [
            jnp.pad(from_low, pad_y_low)[:, None],
            prolong_x,
            jnp.pad(from_high, pad_y_high)[:, None],
        ],
        axis=1,
    )

    applied = jnp.dot(stencil_pos, prolong_frame.reshape(32 * width, 9 * width), precision=HI)
    product = lax.dot_general(prolong_own, applied, (((0,), (0,)), ((), ())), precision=HI)
    product = product.reshape(3, 3, width, 3, 3, width)
    product = jnp.pad(product, ((0, 0), (0, 0), (0, 0), (1, 1), (1, 1), (0, 0)))
    lines = []
    for row_x in range(3):
        column = []
        for row_y in range(3):
            piece = product[row_x, row_y, :, row_x : row_x + 3, row_y : row_y + 3, :]
            column.append(piece.reshape(width, 9 * width))
        lines.append(jnp.stack(column))
    partial_rows = jnp.stack(lines)

    acc = partial_rows[1] + shift(partial_rows[2], "gx", True) + shift(partial_rows[0], "gx", False)
    total = acc[1] + shift(acc[2], "gy", True) + shift(acc[0], "gy", False)
    column_mask = jnp.repeat(coarse_pattern[0, 0].astype(jnp.float32), width)[None, :]
    coarse_block = total * column_mask

    slot_row = jnp.broadcast_to(slot.astype(jnp.float32).reshape(1, 1), (1, 9 * width))
    payload = jnp.concatenate([coarse_block, slot_row], axis=0)
    count = lax.axis_size("gx")
    members = [payload]
    for step in (1, 2, 3):
        pairs = [(i, 4 * (i // 4) + (i % 4 + step) % 4) for i in range(count)]
        members.append(lax.ppermute(payload, "gx", pairs))
    grouped = []
    for target in range(4):
        chosen = jnp.zeros_like(coarse_block)
        for member in members:
            chosen = jnp.where(member[width:, :1] == float(target), member[:width], chosen)
        grouped.append(chosen)
    grouped = jnp.stack(grouped)
    return (coarse_block[None, None], grouped[None, None])


def solution(mesh):
    placed = (
        P("gx", "gy", None, None, None),
        P("gx", "gy", None, None),
        P("gx", "gy", None, None, None),
        P("gx", "gy", None, None, None),
        P("gx", "gy", None),
        P("gx", "gy"),
    )
    return jax.shard_map(
        local,
        mesh=mesh,
        in_specs=placed,
        out_specs=(P("gx", "gy", None, None), P("gx", "gy", None, None, None)),
        check_vma=False,
    )
```

```python
import jax
import jax.numpy as jnp
import numpy as np
from jax import lax
from jax.sharding import PartitionSpec as P

OMEGA = 0.6
HI = lax.Precision.HIGHEST


def shift(block, axis, forward):
    count = lax.axis_size(axis)
    if forward:
        pairs = [(i, i + 1) for i in range(count - 1)]
    else:
        pairs = [(i + 1, i) for i in range(count - 1)]
    return lax.ppermute(block, axis, pairs)


def offset_number(shift_x, shift_y, shift_z):
    return 9 * (shift_x + 1) + 3 * (shift_y + 1) + (shift_z + 1)


POSITIONS = [(pos_x, pos_y, pos_z) for pos_x in range(4) for pos_y in range(4) for pos_z in range(2)]
CELLS = [(cell_x, cell_y, cell_z) for cell_x in range(2) for cell_y in range(2) for cell_z in range(2)]
REACH = [0, 1, 1, 2]


def to_positions(rows):
    width = rows.shape[-1] // 27
    lines = []
    for cell in CELLS:
        block = rows[cell]
        pieces = []
        for pos_x, pos_y, pos_z in POSITIONS:
            shift_x, shift_y, shift_z = pos_x - 1 - cell[0], pos_y - 1 - cell[1], pos_z - cell[2]
            if max(abs(shift_x), abs(shift_y), abs(shift_z)) <= 1:
                number = offset_number(shift_x, shift_y, shift_z)
                pieces.append(block[:, number * width : (number + 1) * width])
            else:
                pieces.append(jnp.zeros((block.shape[0], width), block.dtype))
        lines.append(jnp.concatenate(pieces, axis=1))
    return jnp.concatenate(lines, axis=0)


def local(stencil, pattern, tentative, diag_inverse, coarse_pattern, slot):
    width = tentative.shape[-1]
    zeros = jnp.zeros((width, width), jnp.float32)
    keep_mask = jnp.repeat(pattern.astype(jnp.float32), width, axis=-1)[:, :, :, None, :]
    stencil_rows = stencil * keep_mask
    scaled_rows = jnp.einsum("xyzrs,xyzsk->xyzrk", diag_inverse, stencil_rows, precision=HI)
    stencil_pos = to_positions(stencil_rows)
    scaled_pos = to_positions(scaled_rows)

    tent = {}
    for cell in CELLS:
        tent[(cell[0] + 1, cell[1] + 1, cell[2])] = tentative[cell]
    left = shift(tentative[1], "gx", True)
    right = shift(tentative[0], "gx", False)
    for cell_y in range(2):
        for cell_z in range(2):
            tent[(0, cell_y + 1, cell_z)] = left[cell_y, cell_z]
            tent[(3, cell_y + 1, cell_z)] = right[cell_y, cell_z]
    send_high = jnp.stack([tent[(pos_x, 2, pos_z)] for pos_x in range(4) for pos_z in range(2)])
    send_low = jnp.stack([tent[(pos_x, 1, pos_z)] for pos_x in range(4) for pos_z in range(2)])
    low = shift(send_high, "gy", True)
    high = shift(send_low, "gy", False)
    for pos_x in range(4):
        for pos_z in range(2):
            tent[(pos_x, 0, pos_z)] = low[2 * pos_x + pos_z]
            tent[(pos_x, 3, pos_z)] = high[2 * pos_x + pos_z]

    tent_rows = []
    for pos in POSITIONS:
        target = 3 * REACH[pos[0]] + REACH[pos[1]]
        tent_rows.append(
            jnp.concatenate([tent[pos] if number == target else zeros for number in range(9)], axis=1)
        )
    tent_agg = jnp.concatenate(tent_rows, axis=0)
    smoothed = jnp.dot(scaled_pos, tent_agg, precision=HI)
    own_tent = jnp.concatenate(
        [
            jnp.concatenate([tentative[cell] if number == 4 else zeros for number in range(9)], axis=1)
            for cell in CELLS
        ],
        axis=0,
    )
    prolong_own = own_tent - OMEGA * smoothed

    prolong = {}
    for number, cell in enumerate(CELLS):
        prolong[(cell[0] + 1, cell[1] + 1, cell[2])] = prolong_own[number * width : (number + 1) * width]
    to_low = jnp.stack([prolong[(1, pos_y, pos_z)][:, : 6 * width] for pos_y in (1, 2) for pos_z in range(2)])
    to_high = jnp.stack([prolong[(2, pos_y, pos_z)][:, 3 * width :] for pos_y in (1, 2) for pos_z in range(2)])
    from_right = shift(to_low, "gx", False)
    from_left = shift(to_high, "gx", True)
    wide_zeros = jnp.zeros((width, 3 * width), jnp.float32)
    for index, (pos_y, pos_z) in enumerate((pos_y, pos_z) for pos_y in (1, 2) for pos_z in range(2)):
        prolong[(3, pos_y, pos_z)] = jnp.concatenate([wide_zeros, from_right[index]], axis=1)
        prolong[(0, pos_y, pos_z)] = jnp.concatenate([from_left[index], wide_zeros], axis=1)

    def keep_y(block, first):
        return jnp.concatenate(
            [block[:, (3 * row + first) * width : (3 * row + first + 2) * width] for row in range(3)], axis=1
        )

    def spread_y(block, first):
        pieces = []
        for row in range(3):
            part = block[:, 2 * row * width : (2 * row + 2) * width]
            pieces.extend([zeros, part] if first == 1 else [part, zeros])
        return jnp.concatenate(pieces, axis=1)

    to_low = jnp.stack([keep_y(prolong[(pos_x, 1, pos_z)], 0) for pos_x in range(4) for pos_z in range(2)])
    to_high = jnp.stack([keep_y(prolong[(pos_x, 2, pos_z)], 1) for pos_x in range(4) for pos_z in range(2)])
    from_high = shift(to_low, "gy", False)
    from_low = shift(to_high, "gy", True)
    for pos_x in range(4):
        for pos_z in range(2):
            prolong[(pos_x, 3, pos_z)] = spread_y(from_high[2 * pos_x + pos_z], 1)
            prolong[(pos_x, 0, pos_z)] = spread_y(from_low[2 * pos_x + pos_z], 0)
    prolong_frame = jnp.concatenate([prolong[pos] for pos in POSITIONS], axis=0)

    applied = jnp.dot(stencil_pos, prolong_frame, precision=HI)
    product = lax.dot_general(prolong_own, applied, (((0,), (0,)), ((), ())), precision=HI)
    partial_rows = []
    for row_x in range(3):
        line = []
        for row_y in range(3):
            rows = product[(3 * row_x + row_y) * width : (3 * row_x + row_y + 1) * width]
            pieces = []
            for shift_x in (-1, 0, 1):
                for shift_y in (-1, 0, 1):
                    col_x, col_y = row_x + shift_x, row_y + shift_y
                    if 0 <= col_x <= 2 and 0 <= col_y <= 2:
                        number = 3 * col_x + col_y
                        pieces.append(rows[:, number * width : (number + 1) * width])
                    else:
                        pieces.append(zeros)
            line.append(jnp.concatenate(pieces, axis=1))
        partial_rows.append(jnp.stack(line))

    acc = partial_rows[1] + shift(partial_rows[2], "gx", True) + shift(partial_rows[0], "gx", False)
    total = acc[1] + shift(acc[2], "gy", True) + shift(acc[0], "gy", False)
    column_mask = jnp.repeat(coarse_pattern[0, 0].astype(jnp.float32), width)[None, :]
    coarse_block = total * column_mask

    slot_row = jnp.broadcast_to(slot.astype(jnp.float32).reshape(1, 1), (1, 9 * width))
    payload = jnp.concatenate([coarse_block, slot_row], axis=0)
    count = lax.axis_size("gx")
    members = [payload]
    for step in (1, 2, 3):
        pairs = [(i, 4 * (i // 4) + (i % 4 + step) % 4) for i in range(count)]
        members.append(lax.ppermute(payload, "gx", pairs))
    grouped = []
    for target in range(4):
        chosen = jnp.zeros_like(coarse_block)
        for member in members:
            chosen = jnp.where(member[width:, :1] == float(target), member[:width], chosen)
        grouped.append(chosen)
    grouped = jnp.stack(grouped)
    return (coarse_block[None, None], grouped[None, None])


def solution(mesh):
    placed = (
        P("gx", "gy", None, None, None),
        P("gx", "gy", None, None),
        P("gx", "gy", None, None, None),
        P("gx", "gy", None, None, None),
        P("gx", "gy", None),
        P("gx", "gy"),
    )
    return jax.shard_map(
        local,
        mesh=mesh,
        in_specs=placed,
        out_specs=(P("gx", "gy", None, None), P("gx", "gy", None, None, None)),
        check_vma=False,
    )
```

```python
import jax
import jax.numpy as jnp
import numpy as np
from jax import lax
from jax.sharding import PartitionSpec as P

OMEGA = 0.6
HI = lax.Precision.HIGHEST


def shift(block, axis, forward):
    count = lax.axis_size(axis)
    if forward:
        pairs = [(i, i + 1) for i in range(count - 1)]
    else:
        pairs = [(i + 1, i) for i in range(count - 1)]
    return lax.ppermute(block, axis, pairs)


def offset_number(shift_x, shift_y, shift_z):
    return 9 * (shift_x + 1) + 3 * (shift_y + 1) + (shift_z + 1)


POSITIONS = [(pos_x, pos_y, pos_z) for pos_x in range(4) for pos_y in range(4) for pos_z in range(2)]
CELLS = [(cell_x, cell_y, cell_z) for cell_x in range(2) for cell_y in range(2) for cell_z in range(2)]
REACH = [0, 1, 1, 2]


def to_positions(rows):
    width = rows.shape[-1] // 27
    lines = []
    for cell in CELLS:
        block = rows[cell]
        pieces = []
        for pos_x, pos_y, pos_z in POSITIONS:
            shift_x, shift_y, shift_z = pos_x - 1 - cell[0], pos_y - 1 - cell[1], pos_z - cell[2]
            if max(abs(shift_x), abs(shift_y), abs(shift_z)) <= 1:
                number = offset_number(shift_x, shift_y, shift_z)
                pieces.append(block[:, number * width : (number + 1) * width])
            else:
                pieces.append(jnp.zeros((block.shape[0], width), block.dtype))
        lines.append(jnp.concatenate(pieces, axis=1))
    return jnp.concatenate(lines, axis=0)


def local(stencil, pattern, tentative, diag_inverse, coarse_pattern, slot):
    width = tentative.shape[-1]
    zeros = jnp.zeros((width, width), jnp.float32)
    keep_mask = jnp.repeat(pattern.astype(jnp.float32), width, axis=-1)[:, :, :, None, :]
    stencil_rows = stencil * keep_mask
    stencil_pos = to_positions(stencil_rows)

    here_x = lax.axis_index("gx")
    here_y = lax.axis_index("gy")
    block_of = np.arange(9 * width) // width
    repeat = jnp.asarray(np.tile(np.eye(width, dtype=np.float32), (1, 9)))

    def column_block(shift_x, shift_y):
        return 3 * ((here_x + shift_x + 3) % 3) + (here_y + shift_y + 3) % 3

    tent = {}
    for cell in CELLS:
        tent[(cell[0] + 1, cell[1] + 1, cell[2])] = tentative[cell]
    left = shift(tentative[1], "gx", True)
    right = shift(tentative[0], "gx", False)
    for cell_y in range(2):
        for cell_z in range(2):
            tent[(0, cell_y + 1, cell_z)] = left[cell_y, cell_z]
            tent[(3, cell_y + 1, cell_z)] = right[cell_y, cell_z]
    send_high = jnp.stack([tent[(pos_x, 2, pos_z)] for pos_x in range(4) for pos_z in range(2)])
    send_low = jnp.stack([tent[(pos_x, 1, pos_z)] for pos_x in range(4) for pos_z in range(2)])
    low = shift(send_high, "gy", True)
    high = shift(send_low, "gy", False)
    for pos_x in range(4):
        for pos_z in range(2):
            tent[(pos_x, 0, pos_z)] = low[2 * pos_x + pos_z]
            tent[(pos_x, 3, pos_z)] = high[2 * pos_x + pos_z]

    tent_frame = jnp.concatenate([tent[pos] for pos in POSITIONS], axis=0)
    reach_x = np.array([REACH[pos[0]] - 1 for pos in POSITIONS])
    reach_y = np.array([REACH[pos[1]] - 1 for pos in POSITIONS])
    target = column_block(reach_x, reach_y)
    agg_mask = (block_of[None, :] == target[:, None]).astype(jnp.float32)
    agg_mask = jnp.broadcast_to(agg_mask[:, None, :], (32, width, 9 * width)).reshape(32 * width, 9 * width)
    tent_agg = jnp.dot(tent_frame, repeat, precision=HI) * agg_mask
    coupled = jnp.dot(stencil_pos, tent_agg, precision=HI).reshape(8, width, 9 * width)
    smoothed = jnp.einsum("crs,csn->crn", diag_inverse.reshape(8, width, width), coupled, precision=HI)
    own_mask = (block_of == column_block(0, 0)).astype(jnp.float32)[None, :]
    own_tent = jnp.dot(tentative.reshape(8 * width, width), repeat, precision=HI) * own_mask
    prolong_own = own_tent - OMEGA * smoothed.reshape(8 * width, 9 * width)

    prolong = {}
    for number, cell in enumerate(CELLS):
        prolong[(cell[0] + 1, cell[1] + 1, cell[2])] = prolong_own[number * width : (number + 1) * width]
    edge = [(pos_y, pos_z) for pos_y in (1, 2) for pos_z in range(2)]
    from_right = shift(jnp.stack([prolong[(1,) + spot] for spot in edge]), "gx", False)
    from_left = shift(jnp.stack([prolong[(2,) + spot] for spot in edge]), "gx", True)
    for index, spot in enumerate(edge):
        prolong[(3,) + spot] = from_right[index]
        prolong[(0,) + spot] = from_left[index]
    row = [(pos_x, pos_z) for pos_x in range(4) for pos_z in range(2)]
    from_high = shift(jnp.stack([prolong[(spot[0], 1, spot[1])] for spot in row]), "gy", False)
    from_low = shift(jnp.stack([prolong[(spot[0], 2, spot[1])] for spot in row]), "gy", True)
    for index, spot in enumerate(row):
        prolong[(spot[0], 3, spot[1])] = from_high[index]
        prolong[(spot[0], 0, spot[1])] = from_low[index]
    prolong_frame = jnp.concatenate([prolong[pos] for pos in POSITIONS], axis=0)

    relative = np.arange(9 * width) // width
    moved = column_block(relative // 3 - 1, relative % 3 - 1)
    lane = np.arange(9 * width) % width
    reorder = ((block_of[:, None] == moved[None, :]) & (lane[:, None] == lane[None, :])).astype(jnp.float32)
    applied = jnp.dot(jnp.dot(stencil_pos, prolong_frame, precision=HI), reorder, precision=HI)
    prolong_rel = jnp.dot(prolong_own, reorder, precision=HI)
    product = lax.dot_general(prolong_rel, applied, (((0,), (0,)), ((), ())), precision=HI)
    partial_rows = []
    for row_x in range(3):
        line = []
        for row_y in range(3):
            rows = product[(3 * row_x + row_y) * width : (3 * row_x + row_y + 1) * width]
            pieces = []
            for shift_x in (-1, 0, 1):
                for shift_y in (-1, 0, 1):
                    col_x, col_y = row_x + shift_x, row_y + shift_y
                    if 0 <= col_x <= 2 and 0 <= col_y <= 2:
                        number = 3 * col_x + col_y
                        pieces.append(rows[:, number * width : (number + 1) * width])
                    else:
                        pieces.append(zeros)
            line.append(jnp.concatenate(pieces, axis=1))
        partial_rows.append(jnp.stack(line))

    acc = partial_rows[1] + shift(partial_rows[2], "gx", True) + shift(partial_rows[0], "gx", False)
    total = acc[1] + shift(acc[2], "gy", True) + shift(acc[0], "gy", False)
    column_mask = jnp.repeat(coarse_pattern[0, 0].astype(jnp.float32), width)[None, :]
    coarse_block = total * column_mask

    slot_row = jnp.broadcast_to(slot.astype(jnp.float32).reshape(1, 1), (1, 9 * width))
    payload = jnp.concatenate([coarse_block, slot_row], axis=0)
    count = lax.axis_size("gx")
    members = [payload]
    for step in (1, 2, 3):
        pairs = [(i, 4 * (i // 4) + (i % 4 + step) % 4) for i in range(count)]
        members.append(lax.ppermute(payload, "gx", pairs))
    grouped = []
    for target in range(4):
        chosen = jnp.zeros_like(coarse_block)
        for member in members:
            chosen = jnp.where(member[width:, :1] == float(target), member[:width], chosen)
        grouped.append(chosen)
    grouped = jnp.stack(grouped)
    return (coarse_block[None, None], grouped[None, None])


def solution(mesh):
    placed = (
        P("gx", "gy", None, None, None),
        P("gx", "gy", None, None),
        P("gx", "gy", None, None, None),
        P("gx", "gy", None, None, None),
        P("gx", "gy", None),
        P("gx", "gy"),
    )
    return jax.shard_map(
        local,
        mesh=mesh,
        in_specs=placed,
        out_specs=(P("gx", "gy", None, None), P("gx", "gy", None, None, None)),
        check_vma=False,
    )
```

```python
import jax
import jax.numpy as jnp
import numpy as np
from jax import lax
from jax.sharding import PartitionSpec as P

OMEGA = 0.6
HI = lax.Precision.HIGHEST


def shift(block, axis, forward):
    count = lax.axis_size(axis)
    if forward:
        pairs = [(i, i + 1) for i in range(count - 1)]
    else:
        pairs = [(i + 1, i) for i in range(count - 1)]
    return lax.ppermute(block, axis, pairs)


def offset_number(shift_x, shift_y, shift_z):
    return 9 * (shift_x + 1) + 3 * (shift_y + 1) + (shift_z + 1)


EDGE = [(pos_y, pos_z) for pos_y in (1, 2) for pos_z in range(2)]
ROW = [(pos_x, pos_z) for pos_x in range(4) for pos_z in range(2)]
GROUPS = [
    [(cell_x + 1, cell_y + 1, cell_z) for cell_x in range(2) for cell_y in range(2) for cell_z in range(2)],
    [(0,) + spot for spot in EDGE],
    [(3,) + spot for spot in EDGE],
    [(spot[0], 0, spot[1]) for spot in ROW],
    [(spot[0], 3, spot[1]) for spot in ROW],
]
POSITIONS = [pos for group in GROUPS for pos in group]
CELLS = [(cell_x, cell_y, cell_z) for cell_x in range(2) for cell_y in range(2) for cell_z in range(2)]
REACH = [0, 1, 1, 2]


def to_positions(rows):
    width = rows.shape[-1] // 27
    lines = []
    for cell in CELLS:
        block = rows[cell]
        pieces = []
        for pos_x, pos_y, pos_z in POSITIONS:
            shift_x, shift_y, shift_z = pos_x - 1 - cell[0], pos_y - 1 - cell[1], pos_z - cell[2]
            if max(abs(shift_x), abs(shift_y), abs(shift_z)) <= 1:
                number = offset_number(shift_x, shift_y, shift_z)
                pieces.append(block[:, number * width : (number + 1) * width])
            else:
                pieces.append(jnp.zeros((block.shape[0], width), block.dtype))
        lines.append(jnp.concatenate(pieces, axis=1))
    return jnp.concatenate(lines, axis=0)


def local(stencil, pattern, tentative, diag_inverse, coarse_pattern, slot):
    width = tentative.shape[-1]
    zeros = jnp.zeros((width, width), jnp.float32)
    keep_mask = jnp.repeat(pattern.astype(jnp.float32), width, axis=-1)[:, :, :, None, :]
    stencil_rows = stencil * keep_mask
    stencil_pos = to_positions(stencil_rows)

    here_x = lax.axis_index("gx")
    here_y = lax.axis_index("gy")
    block_of = np.arange(9 * width) // width
    repeat = jnp.asarray(np.tile(np.eye(width, dtype=np.float32), (1, 9)))

    def column_block(shift_x, shift_y):
        return 3 * ((here_x + shift_x + 3) % 3) + (here_y + shift_y + 3) % 3

    tent = {}
    for cell in CELLS:
        tent[(cell[0] + 1, cell[1] + 1, cell[2])] = tentative[cell]
    left = shift(tentative[1], "gx", True)
    right = shift(tentative[0], "gx", False)
    for cell_y in range(2):
        for cell_z in range(2):
            tent[(0, cell_y + 1, cell_z)] = left[cell_y, cell_z]
            tent[(3, cell_y + 1, cell_z)] = right[cell_y, cell_z]
    send_high = jnp.stack([tent[(pos_x, 2, pos_z)] for pos_x in range(4) for pos_z in range(2)])
    send_low = jnp.stack([tent[(pos_x, 1, pos_z)] for pos_x in range(4) for pos_z in range(2)])
    low = shift(send_high, "gy", True)
    high = shift(send_low, "gy", False)
    for pos_x in range(4):
        for pos_z in range(2):
            tent[(pos_x, 0, pos_z)] = low[2 * pos_x + pos_z]
            tent[(pos_x, 3, pos_z)] = high[2 * pos_x + pos_z]

    tent_frame = jnp.concatenate([tent[pos] for pos in POSITIONS], axis=0)
    reach_x = np.array([REACH[pos[0]] - 1 for pos in POSITIONS])
    reach_y = np.array([REACH[pos[1]] - 1 for pos in POSITIONS])
    target = column_block(reach_x, reach_y)
    agg_mask = (block_of[None, :] == target[:, None]).astype(jnp.float32)
    agg_mask = jnp.broadcast_to(agg_mask[:, None, :], (32, width, 9 * width)).reshape(32 * width, 9 * width)
    tent_agg = jnp.dot(tent_frame, repeat, precision=HI) * agg_mask
    coupled = jnp.dot(stencil_pos, tent_agg, precision=HI).reshape(8, width, 9 * width)
    smoothed = jnp.einsum("crs,csn->crn", diag_inverse.reshape(8, width, width), coupled, precision=HI)
    own_mask = (block_of == column_block(0, 0)).astype(jnp.float32)[None, :]
    own_tent = jnp.dot(tentative.reshape(8 * width, width), repeat, precision=HI) * own_mask
    prolong_own = own_tent - OMEGA * smoothed.reshape(8 * width, 9 * width)

    prolong = {}
    for number, cell in enumerate(CELLS):
        prolong[(cell[0] + 1, cell[1] + 1, cell[2])] = prolong_own[number * width : (number + 1) * width]
    from_right = shift(jnp.stack([prolong[(1,) + spot] for spot in EDGE]), "gx", False)
    from_left = shift(jnp.stack([prolong[(2,) + spot] for spot in EDGE]), "gx", True)
    for index, spot in enumerate(EDGE):
        prolong[(3,) + spot] = from_right[index]
        prolong[(0,) + spot] = from_left[index]
    from_high = shift(jnp.stack([prolong[(spot[0], 1, spot[1])] for spot in ROW]), "gy", False)
    from_low = shift(jnp.stack([prolong[(spot[0], 2, spot[1])] for spot in ROW]), "gy", True)
    parts = [prolong_own, from_left, from_right, from_low, from_high]
    applied = None
    first = 0
    for group, part in zip(GROUPS, parts):
        last = first + len(group) * width
        term = jnp.dot(stencil_pos[:, first:last], part.reshape(len(group) * width, -1), precision=HI)
        applied = term if applied is None else applied + term
        first = last

    relative = np.arange(9 * width) // width
    moved = column_block(relative // 3 - 1, relative % 3 - 1)
    lane = np.arange(9 * width) % width
    reorder = ((block_of[:, None] == moved[None, :]) & (lane[:, None] == lane[None, :])).astype(jnp.float32)
    applied = jnp.dot(applied, reorder, precision=HI)
    prolong_rel = jnp.dot(prolong_own, reorder, precision=HI)
    product = lax.dot_general(prolong_rel, applied, (((0,), (0,)), ((), ())), precision=HI)
    partial_rows = []
    for row_x in range(3):
        line = []
        for row_y in range(3):
            rows = product[(3 * row_x + row_y) * width : (3 * row_x + row_y + 1) * width]
            pieces = []
            for shift_x in (-1, 0, 1):
                for shift_y in (-1, 0, 1):
                    col_x, col_y = row_x + shift_x, row_y + shift_y
                    if 0 <= col_x <= 2 and 0 <= col_y <= 2:
                        number = 3 * col_x + col_y
                        pieces.append(rows[:, number * width : (number + 1) * width])
                    else:
                        pieces.append(zeros)
            line.append(jnp.concatenate(pieces, axis=1))
        partial_rows.append(jnp.stack(line))

    acc = partial_rows[1] + shift(partial_rows[2], "gx", True) + shift(partial_rows[0], "gx", False)
    total = acc[1] + shift(acc[2], "gy", True) + shift(acc[0], "gy", False)
    column_mask = jnp.repeat(coarse_pattern[0, 0].astype(jnp.float32), width)[None, :]
    coarse_block = total * column_mask

    slot_row = jnp.broadcast_to(slot.astype(jnp.float32).reshape(1, 1), (1, 9 * width))
    payload = jnp.concatenate([coarse_block, slot_row], axis=0)
    count = lax.axis_size("gx")
    members = [payload]
    for step in (1, 2, 3):
        pairs = [(i, 4 * (i // 4) + (i % 4 + step) % 4) for i in range(count)]
        members.append(lax.ppermute(payload, "gx", pairs))
    grouped = []
    for target in range(4):
        chosen = jnp.zeros_like(coarse_block)
        for member in members:
            chosen = jnp.where(member[width:, :1] == float(target), member[:width], chosen)
        grouped.append(chosen)
    grouped = jnp.stack(grouped)
    return (coarse_block[None, None], grouped[None, None])


def solution(mesh):
    placed = (
        P("gx", "gy", None, None, None),
        P("gx", "gy", None, None),
        P("gx", "gy", None, None, None),
        P("gx", "gy", None, None, None),
        P("gx", "gy", None),
        P("gx", "gy"),
    )
    return jax.shard_map(
        local,
        mesh=mesh,
        in_specs=placed,
        out_specs=(P("gx", "gy", None, None), P("gx", "gy", None, None, None)),
        check_vma=False,
    )
```

```python
import jax
import jax.numpy as jnp
import numpy as np
from jax import lax
from jax.sharding import PartitionSpec as P

OMEGA = 0.6
HI = lax.Precision.HIGHEST


def shift(block, axis, forward):
    count = lax.axis_size(axis)
    if forward:
        pairs = [(i, i + 1) for i in range(count - 1)]
    else:
        pairs = [(i + 1, i) for i in range(count - 1)]
    return lax.ppermute(block, axis, pairs)


def offset_number(shift_x, shift_y, shift_z):
    return 9 * (shift_x + 1) + 3 * (shift_y + 1) + (shift_z + 1)


EDGE = [(pos_y, pos_z) for pos_y in (1, 2) for pos_z in range(2)]
ROW = [(pos_x, pos_z) for pos_x in range(4) for pos_z in range(2)]
GROUPS = [
    [(cell_x + 1, cell_y + 1, cell_z) for cell_x in range(2) for cell_y in range(2) for cell_z in range(2)],
    [(0,) + spot for spot in EDGE],
    [(3,) + spot for spot in EDGE],
    [(spot[0], 0, spot[1]) for spot in ROW],
    [(spot[0], 3, spot[1]) for spot in ROW],
]
POSITIONS = [pos for group in GROUPS for pos in group]
CELLS = [(cell_x, cell_y, cell_z) for cell_x in range(2) for cell_y in range(2) for cell_z in range(2)]
REACH = [0, 1, 1, 2]


def to_positions(rows):
    width = rows.shape[-1] // 27
    lines = []
    for cell in CELLS:
        block = rows[cell]
        pieces = []
        for pos_x, pos_y, pos_z in POSITIONS:
            shift_x, shift_y, shift_z = pos_x - 1 - cell[0], pos_y - 1 - cell[1], pos_z - cell[2]
            if max(abs(shift_x), abs(shift_y), abs(shift_z)) <= 1:
                number = offset_number(shift_x, shift_y, shift_z)
                pieces.append(block[:, number * width : (number + 1) * width])
            else:
                pieces.append(jnp.zeros((block.shape[0], width), block.dtype))
        lines.append(jnp.concatenate(pieces, axis=1))
    return jnp.concatenate(lines, axis=0)


def local(stencil, pattern, tentative, diag_inverse, coarse_pattern, slot):
    width = tentative.shape[-1]
    zeros = jnp.zeros((width, width), jnp.float32)
    keep_mask = jnp.repeat(pattern.astype(jnp.float32), width, axis=-1)[:, :, :, None, :]
    stencil_rows = stencil * keep_mask
    stencil_pos = to_positions(stencil_rows)

    here_x = lax.axis_index("gx")
    here_y = lax.axis_index("gy")
    block_of = np.arange(9 * width) // width
    repeat = jnp.asarray(np.tile(np.eye(width, dtype=np.float32), (1, 9)))

    def column_block(shift_x, shift_y):
        return 3 * ((here_x + shift_x + 3) % 3) + (here_y + shift_y + 3) % 3

    tent = {}
    for cell in CELLS:
        tent[(cell[0] + 1, cell[1] + 1, cell[2])] = tentative[cell]
    left = shift(tentative[1], "gx", True)
    right = shift(tentative[0], "gx", False)
    for cell_y in range(2):
        for cell_z in range(2):
            tent[(0, cell_y + 1, cell_z)] = left[cell_y, cell_z]
            tent[(3, cell_y + 1, cell_z)] = right[cell_y, cell_z]
    send_high = jnp.stack([tent[(pos_x, 2, pos_z)] for pos_x in range(4) for pos_z in range(2)])
    send_low = jnp.stack([tent[(pos_x, 1, pos_z)] for pos_x in range(4) for pos_z in range(2)])
    low = shift(send_high, "gy", True)
    high = shift(send_low, "gy", False)
    for pos_x in range(4):
        for pos_z in range(2):
            tent[(pos_x, 0, pos_z)] = low[2 * pos_x + pos_z]
            tent[(pos_x, 3, pos_z)] = high[2 * pos_x + pos_z]

    tent_frame = jnp.concatenate([tent[pos] for pos in POSITIONS], axis=0)
    reach_x = np.array([REACH[pos[0]] - 1 for pos in POSITIONS])
    reach_y = np.array([REACH[pos[1]] - 1 for pos in POSITIONS])
    target = column_block(reach_x, reach_y)
    agg_mask = (block_of[None, :] == target[:, None]).astype(jnp.float32)
    agg_mask = jnp.broadcast_to(agg_mask[:, None, :], (32, width, 9 * width)).reshape(32 * width, 9 * width)
    tent_agg = jnp.dot(tent_frame, repeat, precision=HI) * agg_mask
    coupled = jnp.dot(stencil_pos, tent_agg, precision=HI).reshape(8, width, 9 * width)
    smoothed = jnp.einsum("crs,csn->crn", diag_inverse.reshape(8, width, width), coupled, precision=HI)
    own_mask = (block_of == column_block(0, 0)).astype(jnp.float32)[None, :]
    own_tent = jnp.dot(tentative.reshape(8 * width, width), repeat, precision=HI) * own_mask
    prolong_own = own_tent - OMEGA * smoothed.reshape(8 * width, 9 * width)

    prolong = {}
    for number, cell in enumerate(CELLS):
        prolong[(cell[0] + 1, cell[1] + 1, cell[2])] = prolong_own[number * width : (number + 1) * width]
    from_right = shift(jnp.stack([prolong[(1,) + spot] for spot in EDGE]), "gx", False)
    from_left = shift(jnp.stack([prolong[(2,) + spot] for spot in EDGE]), "gx", True)
    for index, spot in enumerate(EDGE):
        prolong[(3,) + spot] = from_right[index]
        prolong[(0,) + spot] = from_left[index]
    from_high = shift(jnp.stack([prolong[(spot[0], 1, spot[1])] for spot in ROW]), "gy", False)
    from_low = shift(jnp.stack([prolong[(spot[0], 2, spot[1])] for spot in ROW]), "gy", True)
    parts = [prolong_own, from_left, from_right, from_low, from_high]
    applied = None
    first = 0
    for group, part in zip(GROUPS, parts):
        last = first + len(group) * width
        term = jnp.dot(stencil_pos[:, first:last], part.reshape(len(group) * width, -1), precision=HI)
        applied = term if applied is None else applied + term
        first = last

    relative = np.arange(9 * width) // width
    moved = column_block(relative // 3 - 1, relative % 3 - 1)
    lane = np.arange(9 * width) % width
    reorder = ((block_of[:, None] == moved[None, :]) & (lane[:, None] == lane[None, :])).astype(jnp.float32)
    applied = jnp.dot(applied, reorder, precision=HI)
    prolong_rel = jnp.dot(prolong_own, reorder, precision=HI)
    product = lax.dot_general(prolong_rel, applied, (((0,), (0,)), ((), ())), precision=HI)
    partial_rows = []
    for row_x in range(3):
        line = []
        for row_y in range(3):
            rows = product[(3 * row_x + row_y) * width : (3 * row_x + row_y + 1) * width]
            pieces = []
            for shift_x in (-1, 0, 1):
                for shift_y in (-1, 0, 1):
                    col_x, col_y = row_x + shift_x, row_y + shift_y
                    if 0 <= col_x <= 2 and 0 <= col_y <= 2:
                        number = 3 * col_x + col_y
                        pieces.append(rows[:, number * width : (number + 1) * width])
                    else:
                        pieces.append(zeros)
            line.append(jnp.concatenate(pieces, axis=1))
        partial_rows.append(jnp.stack(line))

    acc = partial_rows[1] + shift(partial_rows[2], "gx", True) + shift(partial_rows[0], "gx", False)
    total = acc[1] + shift(acc[2], "gy", True) + shift(acc[0], "gy", False)
    column_mask = jnp.repeat(coarse_pattern[0, 0].astype(jnp.float32), width)[None, :]
    coarse_block = total * column_mask

    slot_row = jnp.broadcast_to(slot.astype(jnp.float32).reshape(1, 1), (1, 9 * width))
    payload = jnp.concatenate([coarse_block, slot_row], axis=0)
    count = lax.axis_size("gx")
    held = payload[None]
    for level in (0, 1):
        partner = lax.ppermute(held, "gx", [(i, i ^ (1 << level)) for i in range(count)])
        held = jnp.concatenate([held, partner], axis=0)
    members = [held[index] for index in range(4)]
    grouped = []
    for target in range(4):
        chosen = jnp.zeros_like(coarse_block)
        for member in members:
            chosen = jnp.where(member[width:, :1] == float(target), member[:width], chosen)
        grouped.append(chosen)
    grouped = jnp.stack(grouped)
    return (coarse_block[None, None], grouped[None, None])


def solution(mesh):
    placed = (
        P("gx", "gy", None, None, None),
        P("gx", "gy", None, None),
        P("gx", "gy", None, None, None),
        P("gx", "gy", None, None, None),
        P("gx", "gy", None),
        P("gx", "gy"),
    )
    return jax.shard_map(
        local,
        mesh=mesh,
        in_specs=placed,
        out_specs=(P("gx", "gy", None, None), P("gx", "gy", None, None, None)),
        check_vma=False,
    )
```

```python
import jax
import jax.numpy as jnp
import numpy as np
from jax import lax
from jax.sharding import PartitionSpec as P

OMEGA = 0.6
HI = lax.Precision.HIGHEST


def shift(block, axis, forward):
    count = lax.axis_size(axis)
    if forward:
        pairs = [(i, i + 1) for i in range(count - 1)]
    else:
        pairs = [(i + 1, i) for i in range(count - 1)]
    return lax.ppermute(block, axis, pairs)


def offset_number(shift_x, shift_y, shift_z):
    return 9 * (shift_x + 1) + 3 * (shift_y + 1) + (shift_z + 1)


EDGE = [(pos_y, pos_z) for pos_y in (1, 2) for pos_z in range(2)]
ROW = [(pos_x, pos_z) for pos_x in range(4) for pos_z in range(2)]
GROUPS = [
    [(cell_x + 1, cell_y + 1, cell_z) for cell_x in range(2) for cell_y in range(2) for cell_z in range(2)],
    [(0,) + spot for spot in EDGE],
    [(3,) + spot for spot in EDGE],
    [(spot[0], 0, spot[1]) for spot in ROW],
    [(spot[0], 3, spot[1]) for spot in ROW],
]
POSITIONS = [pos for group in GROUPS for pos in group]
CELLS = [(cell_x, cell_y, cell_z) for cell_x in range(2) for cell_y in range(2) for cell_z in range(2)]
REACH = [0, 1, 1, 2]


def to_positions(rows):
    width = rows.shape[-1] // 27
    lines = []
    for cell in CELLS:
        block = rows[cell]
        pieces = []
        for pos_x, pos_y, pos_z in POSITIONS:
            shift_x, shift_y, shift_z = pos_x - 1 - cell[0], pos_y - 1 - cell[1], pos_z - cell[2]
            if max(abs(shift_x), abs(shift_y), abs(shift_z)) <= 1:
                number = offset_number(shift_x, shift_y, shift_z)
                pieces.append(block[:, number * width : (number + 1) * width])
            else:
                pieces.append(jnp.zeros((block.shape[0], width), block.dtype))
        lines.append(jnp.concatenate(pieces, axis=1))
    return jnp.concatenate(lines, axis=0)


def local(stencil, pattern, tentative, diag_inverse, coarse_pattern, slot):
    width = tentative.shape[-1]
    zeros = jnp.zeros((width, width), jnp.float32)
    keep_mask = jnp.repeat(pattern.astype(jnp.float32), width, axis=-1)[:, :, :, None, :]
    stencil_rows = stencil * keep_mask
    stencil_pos = to_positions(stencil_rows)

    here_x = lax.axis_index("gx")
    here_y = lax.axis_index("gy")
    block_of = np.arange(9 * width) // width
    repeat = jnp.asarray(np.tile(np.eye(width, dtype=np.float32), (1, 9)))

    def column_block(shift_x, shift_y):
        return 3 * ((here_x + shift_x + 3) % 3) + (here_y + shift_y + 3) % 3

    tent = {}
    for cell in CELLS:
        tent[(cell[0] + 1, cell[1] + 1, cell[2])] = tentative[cell]
    left = shift(tentative[1], "gx", True)
    right = shift(tentative[0], "gx", False)
    for cell_y in range(2):
        for cell_z in range(2):
            tent[(0, cell_y + 1, cell_z)] = left[cell_y, cell_z]
            tent[(3, cell_y + 1, cell_z)] = right[cell_y, cell_z]
    send_high = jnp.stack([tent[(pos_x, 2, pos_z)] for pos_x in range(4) for pos_z in range(2)])
    send_low = jnp.stack([tent[(pos_x, 1, pos_z)] for pos_x in range(4) for pos_z in range(2)])
    low = shift(send_high, "gy", True)
    high = shift(send_low, "gy", False)
    for pos_x in range(4):
        for pos_z in range(2):
            tent[(pos_x, 0, pos_z)] = low[2 * pos_x + pos_z]
            tent[(pos_x, 3, pos_z)] = high[2 * pos_x + pos_z]

    tent_frame = jnp.concatenate([tent[pos] for pos in POSITIONS], axis=0)
    reach_x = np.array([REACH[pos[0]] - 1 for pos in POSITIONS])
    reach_y = np.array([REACH[pos[1]] - 1 for pos in POSITIONS])
    target = column_block(reach_x, reach_y)
    agg_mask = (block_of[None, :] == target[:, None]).astype(jnp.float32)
    agg_mask = jnp.broadcast_to(agg_mask[:, None, :], (32, width, 9 * width)).reshape(32 * width, 9 * width)
    tent_agg = jnp.dot(tent_frame, repeat, precision=HI) * agg_mask
    coupled = jnp.dot(stencil_pos, tent_agg, precision=HI).reshape(8, width, 9 * width)
    smoothed = jnp.einsum("crs,csn->crn", diag_inverse.reshape(8, width, width), coupled, precision=HI)
    own_mask = (block_of == column_block(0, 0)).astype(jnp.float32)[None, :]
    own_tent = jnp.dot(tentative.reshape(8 * width, width), repeat, precision=HI) * own_mask
    prolong_own = own_tent - OMEGA * smoothed.reshape(8 * width, 9 * width)

    prolong = {}
    for number, cell in enumerate(CELLS):
        prolong[(cell[0] + 1, cell[1] + 1, cell[2])] = prolong_own[number * width : (number + 1) * width]
    from_right = shift(jnp.stack([prolong[(1,) + spot] for spot in EDGE]), "gx", False)
    from_left = shift(jnp.stack([prolong[(2,) + spot] for spot in EDGE]), "gx", True)
    for index, spot in enumerate(EDGE):
        prolong[(3,) + spot] = from_right[index]
        prolong[(0,) + spot] = from_left[index]
    from_high = shift(jnp.stack([prolong[(spot[0], 1, spot[1])] for spot in ROW]), "gy", False)
    from_low = shift(jnp.stack([prolong[(spot[0], 2, spot[1])] for spot in ROW]), "gy", True)
    parts = [prolong_own, from_left, from_right, from_low, from_high]
    applied = None
    first = 0
    for group, part in zip(GROUPS, parts):
        last = first + len(group) * width
        term = jnp.dot(stencil_pos[:, first:last], part.reshape(len(group) * width, -1), precision=HI)
        applied = term if applied is None else applied + term
        first = last

    relative = np.arange(9 * width) // width
    moved = column_block(relative // 3 - 1, relative % 3 - 1)
    lane = np.arange(9 * width) % width
    reorder = ((block_of[:, None] == moved[None, :]) & (lane[:, None] == lane[None, :])).astype(jnp.float32)
    applied = jnp.dot(applied, reorder, precision=HI)
    prolong_rel = jnp.dot(prolong_own, reorder, precision=HI)
    product = lax.dot_general(prolong_rel, applied, (((0,), (0,)), ((), ())), precision=HI)
    partial_rows = []
    for row_x in range(3):
        line = []
        for row_y in range(3):
            rows = product[(3 * row_x + row_y) * width : (3 * row_x + row_y + 1) * width]
            pieces = []
            for shift_x in (-1, 0, 1):
                for shift_y in (-1, 0, 1):
                    col_x, col_y = row_x + shift_x, row_y + shift_y
                    if 0 <= col_x <= 2 and 0 <= col_y <= 2:
                        number = 3 * col_x + col_y
                        pieces.append(rows[:, number * width : (number + 1) * width])
                    else:
                        pieces.append(zeros)
            line.append(jnp.concatenate(pieces, axis=1))
        partial_rows.append(jnp.stack(line))

    partial_rows = jnp.stack(partial_rows)
    acc = partial_rows[:, 1] + shift(partial_rows[:, 2], "gy", True) + shift(partial_rows[:, 0], "gy", False)
    column_mask = jnp.repeat(coarse_pattern[0, 0].astype(jnp.float32), width)[None, :]
    slot_row = jnp.broadcast_to(slot.astype(jnp.float32).reshape(1, 1), (1, 9 * width))
    mine = jnp.concatenate([acc.reshape(3 * width, 9 * width), column_mask, slot_row], axis=0)
    count = lax.axis_size("gx")
    odd = here_x % 2 == 1
    partner = lax.ppermute(mine, "gx", [(i, i ^ 1) for i in range(count)])
    edge_piece = jnp.where(odd, acc[2], acc[0])
    near_pairs = [(i, i + 1 if i % 2 else i - 1) for i in range(count)]
    far_pairs = [(i, i + 2 if i % 2 else i - 2) for i in range(count)]
    near = lax.ppermute(edge_piece, "gx", [pair for pair in near_pairs if 0 <= pair[1] < count])
    far = lax.ppermute(edge_piece, "gx", [pair for pair in far_pairs if 0 <= pair[1] < count])
    before = jnp.where(odd, far, near)
    after = jnp.where(odd, near, far)
    lower = jnp.where(odd, partner, mine)
    upper = jnp.where(odd, mine, partner)

    def rows_of(held, index):
        return held[index * width : (index + 1) * width]

    total_lower = before + rows_of(lower, 1) + rows_of(upper, 0)
    total_upper = rows_of(lower, 2) + rows_of(upper, 1) + after
    coarse_lower = total_lower * lower[3 * width : 3 * width + 1]
    coarse_upper = total_upper * upper[3 * width : 3 * width + 1]
    coarse_block = jnp.where(odd, coarse_upper, coarse_lower)
    held = jnp.stack(
        [
            jnp.concatenate([coarse_lower, lower[3 * width + 1 :]], axis=0),
            jnp.concatenate([coarse_upper, upper[3 * width + 1 :]], axis=0),
        ]
    )
    held = jnp.concatenate([held, lax.ppermute(held, "gx", [(i, i ^ 2) for i in range(count)])], axis=0)
    members = [held[index] for index in range(4)]
    grouped = []
    for target in range(4):
        chosen = jnp.zeros_like(coarse_block)
        for member in members:
            chosen = jnp.where(member[width:, :1] == float(target), member[:width], chosen)
        grouped.append(chosen)
    grouped = jnp.stack(grouped)
    return (coarse_block[None, None], grouped[None, None])


def solution(mesh):
    placed = (
        P("gx", "gy", None, None, None),
        P("gx", "gy", None, None),
        P("gx", "gy", None, None, None),
        P("gx", "gy", None, None, None),
        P("gx", "gy", None),
        P("gx", "gy"),
    )
    return jax.shard_map(
        local,
        mesh=mesh,
        in_specs=placed,
        out_specs=(P("gx", "gy", None, None), P("gx", "gy", None, None, None)),
        check_vma=False,
    )
```

```python
import jax
import jax.numpy as jnp
import numpy as np
from jax import lax
from jax.sharding import PartitionSpec as P

OMEGA = 0.6
HI = lax.Precision.HIGHEST


def shift(block, axis, forward):
    count = lax.axis_size(axis)
    if forward:
        pairs = [(i, i + 1) for i in range(count - 1)]
    else:
        pairs = [(i + 1, i) for i in range(count - 1)]
    return lax.ppermute(block, axis, pairs)


def offset_number(shift_x, shift_y, shift_z):
    return 9 * (shift_x + 1) + 3 * (shift_y + 1) + (shift_z + 1)


EDGE = [(pos_y, pos_z) for pos_y in (1, 2) for pos_z in range(2)]
ROW = [(pos_x, pos_z) for pos_x in range(4) for pos_z in range(2)]
GROUPS = [
    [(cell_x + 1, cell_y + 1, cell_z) for cell_x in range(2) for cell_y in range(2) for cell_z in range(2)],
    [(0,) + spot for spot in EDGE],
    [(3,) + spot for spot in EDGE],
    [(spot[0], 0, spot[1]) for spot in ROW],
    [(spot[0], 3, spot[1]) for spot in ROW],
]
POSITIONS = [pos for group in GROUPS for pos in group]
CELLS = [(cell_x, cell_y, cell_z) for cell_x in range(2) for cell_y in range(2) for cell_z in range(2)]
REACH = [0, 1, 1, 2]


def to_positions(rows):
    width = rows.shape[-1] // 27
    lines = []
    for cell in CELLS:
        block = rows[cell]
        pieces = []
        for pos_x, pos_y, pos_z in POSITIONS:
            shift_x, shift_y, shift_z = pos_x - 1 - cell[0], pos_y - 1 - cell[1], pos_z - cell[2]
            if max(abs(shift_x), abs(shift_y), abs(shift_z)) <= 1:
                number = offset_number(shift_x, shift_y, shift_z)
                pieces.append(block[:, number * width : (number + 1) * width])
            else:
                pieces.append(jnp.zeros((block.shape[0], width), block.dtype))
        lines.append(jnp.concatenate(pieces, axis=1))
    return jnp.concatenate(lines, axis=0)


def local(stencil, pattern, tentative, diag_inverse, coarse_pattern, slot):
    width = tentative.shape[-1]
    zeros = jnp.zeros((width, width), jnp.float32)
    keep_mask = jnp.repeat(pattern.astype(jnp.float32), width, axis=-1)[:, :, :, None, :]
    stencil_rows = stencil * keep_mask
    stencil_pos = to_positions(stencil_rows)

    here_x = lax.axis_index("gx")
    here_y = lax.axis_index("gy")
    block_of = np.arange(9 * width) // width
    repeat = jnp.asarray(np.tile(np.eye(width, dtype=np.float32), (1, 9)))

    def column_block(shift_x, shift_y):
        return 3 * ((here_x + shift_x + 3) % 3) + (here_y + shift_y + 3) % 3

    tent = {}
    for cell in CELLS:
        tent[(cell[0] + 1, cell[1] + 1, cell[2])] = tentative[cell]
    left = shift(tentative[1], "gx", True)
    right = shift(tentative[0], "gx", False)
    for cell_y in range(2):
        for cell_z in range(2):
            tent[(0, cell_y + 1, cell_z)] = left[cell_y, cell_z]
            tent[(3, cell_y + 1, cell_z)] = right[cell_y, cell_z]
    send_high = jnp.stack([tent[(pos_x, 2, pos_z)] for pos_x in range(4) for pos_z in range(2)])
    send_low = jnp.stack([tent[(pos_x, 1, pos_z)] for pos_x in range(4) for pos_z in range(2)])
    low = shift(send_high, "gy", True)
    high = shift(send_low, "gy", False)
    for pos_x in range(4):
        for pos_z in range(2):
            tent[(pos_x, 0, pos_z)] = low[2 * pos_x + pos_z]
            tent[(pos_x, 3, pos_z)] = high[2 * pos_x + pos_z]

    tent_frame = jnp.concatenate([tent[pos] for pos in POSITIONS], axis=0)
    reach_x = np.array([REACH[pos[0]] - 1 for pos in POSITIONS])
    reach_y = np.array([REACH[pos[1]] - 1 for pos in POSITIONS])
    target = column_block(reach_x, reach_y)
    agg_mask = (block_of[None, :] == target[:, None]).astype(jnp.float32)
    agg_mask = jnp.broadcast_to(agg_mask[:, None, :], (32, width, 9 * width)).reshape(32 * width, 9 * width)
    tent_agg = jnp.dot(tent_frame, repeat, precision=HI) * agg_mask
    split = 16 * width
    coupled = jnp.dot(stencil_pos[:, :split], tent_agg[:split], precision=HI) + jnp.dot(
        stencil_pos[:, split:], tent_agg[split:], precision=HI
    )
    coupled = coupled.reshape(8, width, 9 * width)
    smoothed = jnp.einsum("crs,csn->crn", diag_inverse.reshape(8, width, width), coupled, precision=HI)
    own_mask = (block_of == column_block(0, 0)).astype(jnp.float32)[None, :]
    own_tent = jnp.dot(tentative.reshape(8 * width, width), repeat, precision=HI) * own_mask
    prolong_own = own_tent - OMEGA * smoothed.reshape(8 * width, 9 * width)

    prolong = {}
    for number, cell in enumerate(CELLS):
        prolong[(cell[0] + 1, cell[1] + 1, cell[2])] = prolong_own[number * width : (number + 1) * width]
    from_right = shift(jnp.stack([prolong[(1,) + spot] for spot in EDGE]), "gx", False)
    from_left = shift(jnp.stack([prolong[(2,) + spot] for spot in EDGE]), "gx", True)
    for index, spot in enumerate(EDGE):
        prolong[(3,) + spot] = from_right[index]
        prolong[(0,) + spot] = from_left[index]
    from_high = shift(jnp.stack([prolong[(spot[0], 1, spot[1])] for spot in ROW]), "gy", False)
    from_low = shift(jnp.stack([prolong[(spot[0], 2, spot[1])] for spot in ROW]), "gy", True)
    parts = [prolong_own, from_left, from_right, from_low, from_high]
    terms = []
    first = 0
    for group, part in zip(GROUPS, parts):
        last = first + len(group) * width
        terms.append(jnp.dot(stencil_pos[:, first:last], part.reshape(len(group) * width, -1), precision=HI))
        first = last
    applied_early = terms[0] + terms[1] + terms[2]
    applied_late = terms[3] + terms[4]

    relative = np.arange(9 * width) // width
    moved = column_block(relative // 3 - 1, relative % 3 - 1)
    lane = np.arange(9 * width) % width
    reorder = ((block_of[:, None] == moved[None, :]) & (lane[:, None] == lane[None, :])).astype(jnp.float32)
    prolong_rel = jnp.dot(prolong_own, reorder, precision=HI)
    product = None
    for applied in (applied_early, applied_late):
        applied = jnp.dot(applied, reorder, precision=HI)
        term = lax.dot_general(prolong_rel, applied, (((0,), (0,)), ((), ())), precision=HI)
        product = term if product is None else product + term
    partial_rows = []
    for row_x in range(3):
        line = []
        for row_y in range(3):
            rows = product[(3 * row_x + row_y) * width : (3 * row_x + row_y + 1) * width]
            pieces = []
            for shift_x in (-1, 0, 1):
                for shift_y in (-1, 0, 1):
                    col_x, col_y = row_x + shift_x, row_y + shift_y
                    if 0 <= col_x <= 2 and 0 <= col_y <= 2:
                        number = 3 * col_x + col_y
                        pieces.append(rows[:, number * width : (number + 1) * width])
                    else:
                        pieces.append(zeros)
            line.append(jnp.concatenate(pieces, axis=1))
        partial_rows.append(jnp.stack(line))

    acc = partial_rows[1] + shift(partial_rows[2], "gx", True) + shift(partial_rows[0], "gx", False)
    total = acc[1] + shift(acc[2], "gy", True) + shift(acc[0], "gy", False)
    column_mask = jnp.repeat(coarse_pattern[0, 0].astype(jnp.float32), width)[None, :]
    coarse_block = total * column_mask

    slot_row = jnp.broadcast_to(slot.astype(jnp.float32).reshape(1, 1), (1, 9 * width))
    payload = jnp.concatenate([coarse_block, slot_row], axis=0)
    count = lax.axis_size("gx")
    held = payload[None]
    for level in (0, 1):
        partner = lax.ppermute(held, "gx", [(i, i ^ (1 << level)) for i in range(count)])
        held = jnp.concatenate([held, partner], axis=0)
    members = [held[index] for index in range(4)]
    grouped = []
    for target in range(4):
        chosen = jnp.zeros_like(coarse_block)
        for member in members:
            chosen = jnp.where(member[width:, :1] == float(target), member[:width], chosen)
        grouped.append(chosen)
    grouped = jnp.stack(grouped)
    return (coarse_block[None, None], grouped[None, None])


def solution(mesh):
    placed = (
        P("gx", "gy", None, None, None),
        P("gx", "gy", None, None),
        P("gx", "gy", None, None, None),
        P("gx", "gy", None, None, None),
        P("gx", "gy", None),
        P("gx", "gy"),
    )
    return jax.shard_map(
        local,
        mesh=mesh,
        in_specs=placed,
        out_specs=(P("gx", "gy", None, None), P("gx", "gy", None, None, None)),
        check_vma=False,
    )
```

```python
import jax
import jax.numpy as jnp
import numpy as np
from jax import lax
from jax.sharding import PartitionSpec as P

OMEGA = 0.6
HI = lax.Precision.HIGHEST


def shift(block, axis, forward):
    count = lax.axis_size(axis)
    if forward:
        pairs = [(i, i + 1) for i in range(count - 1)]
    else:
        pairs = [(i + 1, i) for i in range(count - 1)]
    return lax.ppermute(block, axis, pairs)


def offset_number(shift_x, shift_y, shift_z):
    return 9 * (shift_x + 1) + 3 * (shift_y + 1) + (shift_z + 1)


EDGE = [(pos_y, pos_z) for pos_y in (1, 2) for pos_z in range(2)]
ROW = [(pos_x, pos_z) for pos_x in range(4) for pos_z in range(2)]
GROUPS = [
    [(cell_x + 1, cell_y + 1, cell_z) for cell_x in range(2) for cell_y in range(2) for cell_z in range(2)],
    [(0,) + spot for spot in EDGE],
    [(3,) + spot for spot in EDGE],
    [(spot[0], 0, spot[1]) for spot in ROW],
    [(spot[0], 3, spot[1]) for spot in ROW],
]
POSITIONS = [pos for group in GROUPS for pos in group]
CELLS = [(cell_x, cell_y, cell_z) for cell_x in range(2) for cell_y in range(2) for cell_z in range(2)]
REACH = [0, 1, 1, 2]


def to_positions(rows):
    width = rows.shape[-1] // 27
    lines = []
    for cell in CELLS:
        block = rows[cell]
        pieces = []
        for pos_x, pos_y, pos_z in POSITIONS:
            shift_x, shift_y, shift_z = pos_x - 1 - cell[0], pos_y - 1 - cell[1], pos_z - cell[2]
            if max(abs(shift_x), abs(shift_y), abs(shift_z)) <= 1:
                number = offset_number(shift_x, shift_y, shift_z)
                pieces.append(block[:, number * width : (number + 1) * width])
            else:
                pieces.append(jnp.zeros((block.shape[0], width), block.dtype))
        lines.append(jnp.concatenate(pieces, axis=1))
    return jnp.concatenate(lines, axis=0)


def local(stencil, pattern, tentative, diag_inverse, coarse_pattern, slot):
    width = tentative.shape[-1]
    zeros = jnp.zeros((width, width), jnp.float32)
    keep_mask = jnp.repeat(pattern.astype(jnp.float32), width, axis=-1)[:, :, :, None, :]
    stencil_rows = stencil * keep_mask
    stencil_pos = to_positions(stencil_rows)

    here_x = lax.axis_index("gx")
    here_y = lax.axis_index("gy")
    block_of = np.arange(9 * width) // width
    repeat = jnp.asarray(np.tile(np.eye(width, dtype=np.float32), (1, 9)))

    def column_block(shift_x, shift_y):
        return 3 * ((here_x + shift_x + 3) % 3) + (here_y + shift_y + 3) % 3

    tent = {}
    for cell in CELLS:
        tent[(cell[0] + 1, cell[1] + 1, cell[2])] = tentative[cell]
    count_x, count_y = lax.axis_size("gx"), lax.axis_size("gy")

    def from_neighbour(block, step_x, step_y):
        pairs = []
        for source_x in range(count_x):
            for source_y in range(count_y):
                target_x, target_y = source_x + step_x, source_y + step_y
                if 0 <= target_x < count_x and 0 <= target_y < count_y:
                    pairs.append((source_x * count_y + source_y, target_x * count_y + target_y))
        return lax.ppermute(block, ("gx", "gy"), pairs)

    left = shift(tentative[1], "gx", True)
    right = shift(tentative[0], "gx", False)
    low = shift(tentative[:, 1], "gy", True)
    high = shift(tentative[:, 0], "gy", False)
    corners = {
        (0, 0): from_neighbour(tentative[1, 1], 1, 1),
        (0, 3): from_neighbour(tentative[1, 0], 1, -1),
        (3, 0): from_neighbour(tentative[0, 1], -1, 1),
        (3, 3): from_neighbour(tentative[0, 0], -1, -1),
    }
    for cell_y in range(2):
        for cell_z in range(2):
            tent[(0, cell_y + 1, cell_z)] = left[cell_y, cell_z]
            tent[(3, cell_y + 1, cell_z)] = right[cell_y, cell_z]
    for cell_x in range(2):
        for cell_z in range(2):
            tent[(cell_x + 1, 0, cell_z)] = low[cell_x, cell_z]
            tent[(cell_x + 1, 3, cell_z)] = high[cell_x, cell_z]
    for (pos_x, pos_y), block in corners.items():
        for cell_z in range(2):
            tent[(pos_x, pos_y, cell_z)] = block[cell_z]

    tent_frame = jnp.concatenate([tent[pos] for pos in POSITIONS], axis=0)
    reach_x = np.array([REACH[pos[0]] - 1 for pos in POSITIONS])
    reach_y = np.array([REACH[pos[1]] - 1 for pos in POSITIONS])
    target = column_block(reach_x, reach_y)
    agg_mask = (block_of[None, :] == target[:, None]).astype(jnp.float32)
    agg_mask = jnp.broadcast_to(agg_mask[:, None, :], (32, width, 9 * width)).reshape(32 * width, 9 * width)
    tent_agg = jnp.dot(tent_frame, repeat, precision=HI) * agg_mask
    coupled = jnp.dot(stencil_pos, tent_agg, precision=HI).reshape(8, width, 9 * width)
    smoothed = jnp.einsum("crs,csn->crn", diag_inverse.reshape(8, width, width), coupled, precision=HI)
    own_mask = (block_of == column_block(0, 0)).astype(jnp.float32)[None, :]
    own_tent = jnp.dot(tentative.reshape(8 * width, width), repeat, precision=HI) * own_mask
    prolong_own = own_tent - OMEGA * smoothed.reshape(8 * width, 9 * width)

    prolong = {}
    for number, cell in enumerate(CELLS):
        prolong[(cell[0] + 1, cell[1] + 1, cell[2])] = prolong_own[number * width : (number + 1) * width]
    from_right = shift(jnp.stack([prolong[(1,) + spot] for spot in EDGE]), "gx", False)
    from_left = shift(jnp.stack([prolong[(2,) + spot] for spot in EDGE]), "gx", True)
    for index, spot in enumerate(EDGE):
        prolong[(3,) + spot] = from_right[index]
        prolong[(0,) + spot] = from_left[index]
    from_high = shift(jnp.stack([prolong[(spot[0], 1, spot[1])] for spot in ROW]), "gy", False)
    from_low = shift(jnp.stack([prolong[(spot[0], 2, spot[1])] for spot in ROW]), "gy", True)
    parts = [prolong_own, from_left, from_right, from_low, from_high]
    applied = None
    first = 0
    for group, part in zip(GROUPS, parts):
        last = first + len(group) * width
        term = jnp.dot(stencil_pos[:, first:last], part.reshape(len(group) * width, -1), precision=HI)
        applied = term if applied is None else applied + term
        first = last

    relative = np.arange(9 * width) // width
    moved = column_block(relative // 3 - 1, relative % 3 - 1)
    lane = np.arange(9 * width) % width
    reorder = ((block_of[:, None] == moved[None, :]) & (lane[:, None] == lane[None, :])).astype(jnp.float32)
    applied = jnp.dot(applied, reorder, precision=HI)
    prolong_rel = jnp.dot(prolong_own, reorder, precision=HI)
    product = lax.dot_general(prolong_rel, applied, (((0,), (0,)), ((), ())), precision=HI)
    partial_rows = []
    for row_x in range(3):
        line = []
        for row_y in range(3):
            rows = product[(3 * row_x + row_y) * width : (3 * row_x + row_y + 1) * width]
            pieces = []
            for shift_x in (-1, 0, 1):
                for shift_y in (-1, 0, 1):
                    col_x, col_y = row_x + shift_x, row_y + shift_y
                    if 0 <= col_x <= 2 and 0 <= col_y <= 2:
                        number = 3 * col_x + col_y
                        pieces.append(rows[:, number * width : (number + 1) * width])
                    else:
                        pieces.append(zeros)
            line.append(jnp.concatenate(pieces, axis=1))
        partial_rows.append(jnp.stack(line))

    acc = partial_rows[1] + shift(partial_rows[2], "gx", True) + shift(partial_rows[0], "gx", False)
    total = acc[1] + shift(acc[2], "gy", True) + shift(acc[0], "gy", False)
    column_mask = jnp.repeat(coarse_pattern[0, 0].astype(jnp.float32), width)[None, :]
    coarse_block = total * column_mask

    slot_row = jnp.broadcast_to(slot.astype(jnp.float32).reshape(1, 1), (1, 9 * width))
    payload = jnp.concatenate([coarse_block, slot_row], axis=0)
    count = lax.axis_size("gx")
    held = payload[None]
    for level in (0, 1):
        partner = lax.ppermute(held, "gx", [(i, i ^ (1 << level)) for i in range(count)])
        held = jnp.concatenate([held, partner], axis=0)
    members = [held[index] for index in range(4)]
    grouped = []
    for target in range(4):
        chosen = jnp.zeros_like(coarse_block)
        for member in members:
            chosen = jnp.where(member[width:, :1] == float(target), member[:width], chosen)
        grouped.append(chosen)
    grouped = jnp.stack(grouped)
    return (coarse_block[None, None], grouped[None, None])


def solution(mesh):
    placed = (
        P("gx", "gy", None, None, None),
        P("gx", "gy", None, None),
        P("gx", "gy", None, None, None),
        P("gx", "gy", None, None, None),
        P("gx", "gy", None),
        P("gx", "gy"),
    )
    return jax.shard_map(
        local,
        mesh=mesh,
        in_specs=placed,
        out_specs=(P("gx", "gy", None, None), P("gx", "gy", None, None, None)),
        check_vma=False,
    )
```

```python
import jax
import jax.numpy as jnp
import numpy as np
from jax import lax
from jax.sharding import PartitionSpec as P

OMEGA = 0.6
HI = lax.Precision.HIGHEST


def shift(block, axis, forward):
    count = lax.axis_size(axis)
    if forward:
        pairs = [(i, i + 1) for i in range(count - 1)]
    else:
        pairs = [(i + 1, i) for i in range(count - 1)]
    return lax.ppermute(block, axis, pairs)


def offset_number(shift_x, shift_y, shift_z):
    return 9 * (shift_x + 1) + 3 * (shift_y + 1) + (shift_z + 1)


EDGE = [(pos_y, pos_z) for pos_y in (1, 2) for pos_z in range(2)]
ROW = [(pos_x, pos_z) for pos_x in range(4) for pos_z in range(2)]
GROUPS = [
    [(cell_x + 1, cell_y + 1, cell_z) for cell_x in range(2) for cell_y in range(2) for cell_z in range(2)],
    [(0,) + spot for spot in EDGE],
    [(3,) + spot for spot in EDGE],
    [(spot[0], 0, spot[1]) for spot in ROW],
    [(spot[0], 3, spot[1]) for spot in ROW],
]
POSITIONS = [pos for group in GROUPS for pos in group]
CELLS = [(cell_x, cell_y, cell_z) for cell_x in range(2) for cell_y in range(2) for cell_z in range(2)]
REACH = [0, 1, 1, 2]


def to_positions(rows):
    width = rows.shape[-1] // 27
    lines = []
    for cell in CELLS:
        block = rows[cell]
        pieces = []
        for pos_x, pos_y, pos_z in POSITIONS:
            shift_x, shift_y, shift_z = pos_x - 1 - cell[0], pos_y - 1 - cell[1], pos_z - cell[2]
            if max(abs(shift_x), abs(shift_y), abs(shift_z)) <= 1:
                number = offset_number(shift_x, shift_y, shift_z)
                pieces.append(block[:, number * width : (number + 1) * width])
            else:
                pieces.append(jnp.zeros((block.shape[0], width), block.dtype))
        lines.append(jnp.concatenate(pieces, axis=1))
    return jnp.concatenate(lines, axis=0)


def local(stencil, pattern, tentative, diag_inverse, coarse_pattern, slot):
    width = tentative.shape[-1]
    zeros = jnp.zeros((width, width), jnp.float32)
    keep_mask = jnp.repeat(pattern.astype(jnp.float32), width, axis=-1)[:, :, :, None, :]
    stencil_rows = stencil * keep_mask
    stencil_pos = to_positions(stencil_rows)

    here_x = lax.axis_index("gx")
    here_y = lax.axis_index("gy")
    block_of = np.arange(9 * width) // width
    repeat = jnp.asarray(np.tile(np.eye(width, dtype=np.float32), (1, 9)))

    def column_block(shift_x, shift_y):
        return 3 * ((here_x + shift_x + 3) % 3) + (here_y + shift_y + 3) % 3

    tent = {}
    for cell in CELLS:
        tent[(cell[0] + 1, cell[1] + 1, cell[2])] = tentative[cell]
    left = shift(tentative[1], "gx", True)
    right = shift(tentative[0], "gx", False)
    for cell_y in range(2):
        for cell_z in range(2):
            tent[(0, cell_y + 1, cell_z)] = left[cell_y, cell_z]
            tent[(3, cell_y + 1, cell_z)] = right[cell_y, cell_z]
    send_high = jnp.stack([tent[(pos_x, 2, pos_z)] for pos_x in range(4) for pos_z in range(2)])
    send_low = jnp.stack([tent[(pos_x, 1, pos_z)] for pos_x in range(4) for pos_z in range(2)])
    low = shift(send_high, "gy", True)
    high = shift(send_low, "gy", False)
    for pos_x in range(4):
        for pos_z in range(2):
            tent[(pos_x, 0, pos_z)] = low[2 * pos_x + pos_z]
            tent[(pos_x, 3, pos_z)] = high[2 * pos_x + pos_z]

    tent_frame = jnp.concatenate([tent[pos] for pos in POSITIONS], axis=0)
    reach_x = np.array([REACH[pos[0]] - 1 for pos in POSITIONS])
    reach_y = np.array([REACH[pos[1]] - 1 for pos in POSITIONS])
    target = column_block(reach_x, reach_y)
    agg_mask = (block_of[None, :] == target[:, None]).astype(jnp.float32)
    agg_mask = jnp.broadcast_to(agg_mask[:, None, :], (32, width, 9 * width)).reshape(32 * width, 9 * width)
    tent_agg = jnp.dot(tent_frame, repeat, precision=HI) * agg_mask
    coupled = jnp.dot(stencil_pos, tent_agg, precision=HI).reshape(8, width, 9 * width)
    smoothed = jnp.einsum("crs,csn->crn", diag_inverse.reshape(8, width, width), coupled, precision=HI)
    own_mask = (block_of == column_block(0, 0)).astype(jnp.float32)[None, :]
    own_tent = jnp.dot(tentative.reshape(8 * width, width), repeat, precision=HI) * own_mask
    prolong_own = own_tent - OMEGA * smoothed.reshape(8 * width, 9 * width)

    prolong = {}
    for number, cell in enumerate(CELLS):
        prolong[(cell[0] + 1, cell[1] + 1, cell[2])] = prolong_own[number * width : (number + 1) * width]
    from_right = shift(jnp.stack([prolong[(1,) + spot] for spot in EDGE]), "gx", False)
    from_left = shift(jnp.stack([prolong[(2,) + spot] for spot in EDGE]), "gx", True)
    for index, spot in enumerate(EDGE):
        prolong[(3,) + spot] = from_right[index]
        prolong[(0,) + spot] = from_left[index]
    lane_of = np.arange(9 * width) % width
    narrow = np.arange(4 * width)

    def picker(sender_x, sender_y, first_x, first_y):
        quad_x, quad_y = narrow // width // 2, narrow // width % 2
        chosen = 3 * ((sender_x + first_x + quad_x + 3) % 3) + (sender_y + first_y + quad_y + 3) % 3
        hit = (block_of[:, None] == chosen[None, :]) & (lane_of[:, None] == (narrow % width)[None, :])
        return hit.astype(jnp.float32)

    def narrowed(pos_y, first_y):
        halves = []
        for first_x, xs in ((-1, (0, 1)), (0, (2, 3))):
            rows = jnp.concatenate([prolong[(pos_x, pos_y, pos_z)] for pos_x in xs for pos_z in range(2)], axis=0)
            halves.append(jnp.dot(rows, picker(here_x, here_y, first_x, first_y), precision=HI))
        return jnp.concatenate(halves, axis=0)

    def widened(received, sender_y, first_y):
        halves = []
        for half, first_x in enumerate((-1, 0)):
            rows = received[half * 4 * width : (half + 1) * 4 * width]
            halves.append(jnp.dot(rows, picker(here_x, sender_y, first_x, first_y).T, precision=HI))
        return jnp.concatenate(halves, axis=0)

    from_high = widened(shift(narrowed(1, -1), "gy", False), here_y + 1, -1)
    from_low = widened(shift(narrowed(2, 0), "gy", True), here_y - 1, 0)
    parts = [prolong_own, from_left, from_right, from_low, from_high]
    applied = None
    first = 0
    for group, part in zip(GROUPS, parts):
        last = first + len(group) * width
        term = jnp.dot(stencil_pos[:, first:last], part.reshape(len(group) * width, -1), precision=HI)
        applied = term if applied is None else applied + term
        first = last

    relative = np.arange(9 * width) // width
    moved = column_block(relative // 3 - 1, relative % 3 - 1)
    lane = np.arange(9 * width) % width
    reorder = ((block_of[:, None] == moved[None, :]) & (lane[:, None] == lane[None, :])).astype(jnp.float32)
    applied = jnp.dot(applied, reorder, precision=HI)
    prolong_rel = jnp.dot(prolong_own, reorder, precision=HI)
    product = lax.dot_general(prolong_rel, applied, (((0,), (0,)), ((), ())), precision=HI)
    partial_rows = []
    for row_x in range(3):
        line = []
        for row_y in range(3):
            rows = product[(3 * row_x + row_y) * width : (3 * row_x + row_y + 1) * width]
            pieces = []
            for shift_x in (-1, 0, 1):
                for shift_y in (-1, 0, 1):
                    col_x, col_y = row_x + shift_x, row_y + shift_y
                    if 0 <= col_x <= 2 and 0 <= col_y <= 2:
                        number = 3 * col_x + col_y
                        pieces.append(rows[:, number * width : (number + 1) * width])
                    else:
                        pieces.append(zeros)
            line.append(jnp.concatenate(pieces, axis=1))
        partial_rows.append(jnp.stack(line))

    acc = partial_rows[1] + shift(partial_rows[2], "gx", True) + shift(partial_rows[0], "gx", False)
    total = acc[1] + shift(acc[2], "gy", True) + shift(acc[0], "gy", False)
    column_mask = jnp.repeat(coarse_pattern[0, 0].astype(jnp.float32), width)[None, :]
    coarse_block = total * column_mask

    slot_row = jnp.broadcast_to(slot.astype(jnp.float32).reshape(1, 1), (1, 9 * width))
    payload = jnp.concatenate([coarse_block, slot_row], axis=0)
    count = lax.axis_size("gx")
    held = payload[None]
    for level in (0, 1):
        partner = lax.ppermute(held, "gx", [(i, i ^ (1 << level)) for i in range(count)])
        held = jnp.concatenate([held, partner], axis=0)
    members = [held[index] for index in range(4)]
    grouped = []
    for target in range(4):
        chosen = jnp.zeros_like(coarse_block)
        for member in members:
            chosen = jnp.where(member[width:, :1] == float(target), member[:width], chosen)
        grouped.append(chosen)
    grouped = jnp.stack(grouped)
    return (coarse_block[None, None], grouped[None, None])


def solution(mesh):
    placed = (
        P("gx", "gy", None, None, None),
        P("gx", "gy", None, None),
        P("gx", "gy", None, None, None),
        P("gx", "gy", None, None, None),
        P("gx", "gy", None),
        P("gx", "gy"),
    )
    return jax.shard_map(
        local,
        mesh=mesh,
        in_specs=placed,
        out_specs=(P("gx", "gy", None, None), P("gx", "gy", None, None, None)),
        check_vma=False,
    )
```
